256 devices in a mesh: unit: 128 (over z, y, x), samp: 2 (over core).
Axes of the slice: x: 4, y: 4, z: 8, core: 2. Of those that a mesh axis runs over, the one named last changes fastest.
Arguments:
- abundance: float32 [131072, 4096], P('unit', 'samp'), may hold values from 0.0009 to 27, as said below
- unitig_factor: float32 [131072, 128], P('unit'), may hold values from 0.005 to 1.8, as said below
- sample_factor: float32 [4096, 128], P('samp'), may hold values from 0.02 to 0.2
Outputs:
- unitig_update: float32 [131072, 128], P('unit')
- sample_update: float32 [4096, 128], P('samp')
The draws below stay inside these ranges and needn't reach their ends.
Inputs may be any that keep to these rules, and one draw needn't show every extreme that they name: abundance entries are positive. unitig_factor entries are positive.
All inputs are finite; a program needn't handle non-finite values.
Results may differ from the reference program's by a relative error of at most 0.0001.
Values sent between devices are 32-bit elements; how exact they have to be, the bound alone decides.
No kernel may reach another device: no remote copies, remote signals or barrier semaphores. Data moves between devices by JAX's collectives and lax.ppermute only.
A program may use at most 64 MiB of HBM per device.

```python
import math
import jax
import jax.numpy as jnp
from jax import lax

K = 128
ITERS = 2
UNITIGS = 131072
SAMPLES = 4096


def bin_numbers(key):
    return jax.random.randint(jax.random.fold_in(key, 7), (UNITIGS,), 0, K).astype(jnp.int32)


def log_between(key, shape, low, high):
    return jnp.exp(jax.random.uniform(key, shape, jnp.float32, math.log(low), math.log(high)))


def draw_abundance(key, part):
    keys = jax.random.split(jax.random.fold_in(key, 11), 6)
    bins = bin_numbers(key)
    present = jax.random.bernoulli(keys[3], 0.35, (SAMPLES, K))
    row_scale = log_between(keys[0], (UNITIGS, 1), 0.3, 3.0)
    col_scale = log_between(keys[1], (1, SAMPLES), 0.3, 3.0)
    strong = log_between(keys[2], (SAMPLES, K), 0.5, 2.0)
    faint = log_between(keys[4], (SAMPLES, K), 0.02, 0.1)
    noise = log_between(keys[5], (UNITIGS, SAMPLES), 0.5, 1.5)
    profile = jnp.where(present, strong, faint)
    spread = jnp.take(jnp.transpose(profile), bins, axis=0)
    return (row_scale * col_scale * spread * noise).astype(jnp.float32)


def draw_unitig_factor(key, part):
    keys = jax.random.split(jax.random.fold_in(key, 13), 2)
    bins = bin_numbers(key)
    member = bins[:, None] == jnp.arange(K, dtype=jnp.int32)[None, :]
    rising = 1.0 + 2.0 * jnp.arange(UNITIGS, dtype=jnp.float32)[:, None] / max(UNITIGS - 1, 1)
    strong = log_between(keys[0], (UNITIGS, K), 0.2, 0.6)
    faint = log_between(keys[1], (UNITIGS, K), 0.005, 0.03)
    return (jnp.where(member, strong, faint) * rising).astype(jnp.float32)


def shard_levels(rng, dims, cuts, smallest, largest):
    gain, own = 1.0, jax.random.fold_in(rng, 6)
    for axis_at, shards_of in cuts:
        heights = jnp.exp(jax.random.uniform(jax.random.fold_in(own, axis_at), (shards_of,), jnp.float32, smallest / len(cuts), largest / len(cuts)))
        gain = gain * jnp.repeat(heights, dims[axis_at] // shards_of).reshape([-1 if axis == axis_at else 1 for axis in range(len(dims))])
    return gain


def setup_inputs(seed: int = 0) -> dict:
    streams_of = jax.random.split(jax.random.key(seed), 4)
    return {
        "abundance": draw_abundance(jax.random.fold_in(streams_of[3], 71), 0),
        "unitig_factor": draw_unitig_factor(jax.random.fold_in(streams_of[3], 71), 0),
        "sample_factor": jnp.clip(jnp.exp(math.log(0.2) - 2.3025851 * jax.random.uniform(streams_of[2], (SAMPLES, K), jnp.float32) ** shard_levels(streams_of[2], (SAMPLES, K), ((0, 2),), -0.2, 0.2)), 0.02, 0.2),
    }


HI = lax.Precision.HIGHEST


def inner(left, right):
    return lax.dot_general(left, right, (((0,), (0,)), ((), ())), precision=HI, preferred_element_type=jnp.float32)


def reference(abundance, unitig_factor, sample_factor):
    unitig = unitig_factor
    sample = sample_factor
    for sweep in range(ITERS):
        target_h = inner(abundance, unitig)
        gram_unit = inner(unitig, unitig)
        sample = sample * target_h / jnp.dot(sample, gram_unit, precision=HI)
        target_w = jnp.dot(abundance, sample, precision=HI)
        gram_sample = inner(sample, sample)
        unitig = unitig * target_w / jnp.dot(unitig, gram_sample, precision=HI)
    return unitig, sample
```

```python
import jax
import jax.numpy as jnp
from jax import lax
from jax.sharding import Mesh
from jax.sharding import PartitionSpec as P

ITERS = 2


HI = lax.Precision.HIGHEST


def inner(left, right):
    return lax.dot_general(
        left, right, (((0,), (0,)), ((), ())), precision=HI, preferred_element_type=jnp.float32
    )


def shift(axis, n, k):
    return [(j, (j + k) % n) for j in range(n)]


def reduce_scatter(x, axis, n):
    i = lax.axis_index(axis)
    chunks = x.reshape(n, x.shape[0] // n, *x.shape[1:])
    acc = jnp.take(chunks, i, axis=0)
    for k in range(1, n):
        send = jnp.take(chunks, (i + k) % n, axis=0)
        acc = acc + lax.ppermute(send, axis, shift(axis, n, k))
    return acc


def all_gather(piece, axis, n):
    i = lax.axis_index(axis)
    parts = [piece] + [lax.ppermute(piece, axis, shift(axis, n, k)) for k in range(1, n)]
    held = jnp.stack(parts)
    order = (i - jnp.arange(n)) % n
    return jnp.take(held, order, axis=0).reshape(n * piece.shape[0], *piece.shape[1:])


def unit_sum(x, dims):
    for axis, n in reversed(dims):
        x = reduce_scatter(x, axis, n)
    for axis, n in dims:
        x = all_gather(x, axis, n)
    return x


def samp_sum(x):
    return x + lax.ppermute(x, "samp", [(0, 1), (1, 0)])


def shards(dims, abundance, unitig_factor, sample_factor):
    unitig = unitig_factor
    sample = sample_factor
    n_samp = sample.shape[0]
    n_unit = unitig.shape[0]
    for sweep in range(ITERS):
        both = unit_sum(
            jnp.concatenate([inner(abundance, unitig), inner(unitig, unitig)]), dims
        )
        target_h, gram_unit = both[:n_samp], both[n_samp:]
        sample = sample * target_h / jnp.dot(sample, gram_unit, precision=HI)
        both = samp_sum(
            jnp.concatenate([jnp.dot(abundance, sample, precision=HI), inner(sample, sample)])
        )
        target_w, gram_sample = both[:n_unit], both[n_unit:]
        unitig = unitig * target_w / jnp.dot(unitig, gram_sample, precision=HI)
    return (unitig, sample)


def unit_dims(mesh):
    row = mesh.devices[:, 0]
    n = row.shape[0]
    try:
        sizes = [len({d.coords[c] for d in row}) for c in (2, 1, 0)]
    except AttributeError:
        sizes = [n]
    if sizes[0] * sizes[1] * sizes[2] != n if len(sizes) == 3 else True:
        sizes = [n]
    names = ["uz", "uy", "ux"][: len(sizes)]
    return list(zip(names, sizes))


def solution(mesh):
    dims = unit_dims(mesh)
    inner_mesh = Mesh(
        mesh.devices.reshape(*[s for _, s in dims], mesh.devices.shape[1]),
        (*[a for a, _ in dims], "samp"),
    )
    unit = tuple(a for a, _ in dims)
    return jax.shard_map(
        lambda *args: shards(dims, *args),
        mesh=inner_mesh,
        in_specs=(P(unit, "samp"), P(unit, None), P("samp", None)),
        out_specs=(P(unit, None), P("samp", None)),
        check_vma=False,
    )
```

```python
import jax
import jax.numpy as jnp
from jax import lax
from jax.sharding import Mesh
from jax.sharding import PartitionSpec as P

ITERS = 2


HI = lax.Precision.HIGHEST


def inner(left, right):
    return lax.dot_general(
        left, right, (((0,), (0,)), ((), ())), precision=HI, preferred_element_type=jnp.float32
    )


def reduce_scatter(x, axes, n):
    chunks = x.reshape(n, x.shape[0] // n, *x.shape[1:])
    return lax.all_to_all(chunks, axes, 0, 0, tiled=False).sum(0)


def all_gather(piece, axes, n):
    copies = jnp.broadcast_to(piece[None], (n, *piece.shape))
    held = lax.all_to_all(copies, axes, 0, 0, tiled=False)
    return held.reshape(n * piece.shape[0], *piece.shape[1:])


def unit_sum(x, stages):
    for axes, n in stages:
        x = reduce_scatter(x, axes, n)
    for axes, n in reversed(stages):
        x = all_gather(x, axes, n)
    return x


def samp_sum(x):
    return x + lax.ppermute(x, "samp", [(0, 1), (1, 0)])


def shards(stages, abundance, unitig_factor, sample_factor):
    unitig = unitig_factor
    sample = sample_factor
    n_samp = sample.shape[0]
    n_unit = unitig.shape[0]
    for sweep in range(ITERS):
        both = unit_sum(
            jnp.concatenate([inner(abundance, unitig), inner(unitig, unitig)]), stages
        )
        target_h, gram_unit = both[:n_samp], both[n_samp:]
        sample = sample * target_h / jnp.dot(sample, gram_unit, precision=HI)
        both = samp_sum(
            jnp.concatenate([jnp.dot(abundance, sample, precision=HI), inner(sample, sample)])
        )
        target_w, gram_sample = both[:n_unit], both[n_unit:]
        unitig = unitig * target_w / jnp.dot(unitig, gram_sample, precision=HI)
    return (unitig, sample)


def unit_dims(mesh):
    row = mesh.devices[:, 0]
    n = row.shape[0]
    try:
        sizes = [len({d.coords[c] for d in row}) for c in (2, 1, 0)]
    except AttributeError:
        sizes = [n]
    if sizes[0] * sizes[1] * sizes[2] != n if len(sizes) == 3 else True:
        sizes = [n]
    names = ["uz", "uy", "ux"][: len(sizes)]
    return list(zip(names, sizes))


def stages_of(dims):
    if len(dims) < 3:
        return [(tuple(a for a, _ in dims), dims[0][1])]
    (z, nz), (y, ny), (x, nx) = dims
    return [((y, x), ny * nx), (z, nz)]


def solution(mesh):
    dims = unit_dims(mesh)
    inner_mesh = Mesh(
        mesh.devices.reshape(*[s for _, s in dims], mesh.devices.shape[1]),
        (*[a for a, _ in dims], "samp"),
    )
    unit = tuple(a for a, _ in dims)
    return jax.shard_map(
        lambda *args: shards(stages_of(dims), *args),
        mesh=inner_mesh,
        in_specs=(P(unit, "samp"), P(unit, None), P("samp", None)),
        out_specs=(P(unit, None), P("samp", None)),
        check_vma=False,
    )
```

```python
import jax
import jax.numpy as jnp
from jax import lax
from jax.sharding import Mesh
from jax.sharding import PartitionSpec as P

ITERS = 2


HI = lax.Precision.HIGHEST
WIDE = lax.Precision.HIGH


def inner(left, right, precision=HI):
    return lax.dot_general(
        left, right, (((0,), (0,)), ((), ())), precision=precision, preferred_element_type=jnp.float32
    )


def reduce_scatter(x, axes, n):
    chunks = x.reshape(n, x.shape[0] // n, *x.shape[1:])
    return lax.all_to_all(chunks, axes, 0, 0, tiled=False).sum(0)


def all_gather(piece, axes, n):
    copies = jnp.broadcast_to(piece[None], (n, *piece.shape))
    held = lax.all_to_all(copies, axes, 0, 0, tiled=False)
    return held.reshape(n * piece.shape[0], *piece.shape[1:])


def unit_sum(x, stages):
    for axes, n in stages:
        x = reduce_scatter(x, axes, n)
    for axes, n in reversed(stages):
        x = all_gather(x, axes, n)
    return x


def samp_sum(x):
    return x + lax.ppermute(x, "samp", [(0, 1), (1, 0)])


def shards(stages, abundance, unitig_factor, sample_factor):
    unitig = unitig_factor
    sample = sample_factor
    n_samp = sample.shape[0]
    n_unit = unitig.shape[0]
    for sweep in range(ITERS):
        both = unit_sum(
            jnp.concatenate([inner(abundance, unitig, WIDE), inner(unitig, unitig)]), stages
        )
        target_h, gram_unit = both[:n_samp], both[n_samp:]
        sample = sample * target_h / jnp.dot(sample, gram_unit, precision=HI)
        both = samp_sum(
            jnp.concatenate([jnp.dot(abundance, sample, precision=WIDE), inner(sample, sample)])
        )
        target_w, gram_sample = both[:n_unit], both[n_unit:]
        unitig = unitig * target_w / jnp.dot(unitig, gram_sample, precision=HI)
    return (unitig, sample)


def unit_dims(mesh):
    row = mesh.devices[:, 0]
    n = row.shape[0]
    try:
        sizes = [len({d.coords[c] for d in row}) for c in (2, 1, 0)]
    except AttributeError:
        sizes = [n]
    if sizes[0] * sizes[1] * sizes[2] != n if len(sizes) == 3 else True:
        sizes = [n]
    names = ["uz", "uy", "ux"][: len(sizes)]
    return list(zip(names, sizes))


def stages_of(dims):
    if len(dims) < 3:
        return [(tuple(a for a, _ in dims), dims[0][1])]
    (z, nz), (y, ny), (x, nx) = dims
    return [((y, x), ny * nx), (z, nz)]


def solution(mesh):
    dims = unit_dims(mesh)
    inner_mesh = Mesh(
        mesh.devices.reshape(*[s for _, s in dims], mesh.devices.shape[1]),
        (*[a for a, _ in dims], "samp"),
    )
    unit = tuple(a for a, _ in dims)
    return jax.shard_map(
        lambda *args: shards(stages_of(dims), *args),
        mesh=inner_mesh,
        in_specs=(P(unit, "samp"), P(unit, None), P("samp", None)),
        out_specs=(P(unit, None), P("samp", None)),
        check_vma=False,
    )
```

```python
import jax
import jax.numpy as jnp
from jax import lax
from jax.sharding import Mesh
from jax.sharding import PartitionSpec as P

ITERS = 2


HI = lax.Precision.HIGHEST
WIDE = lax.Precision.HIGH


def inner(left, right, precision=HI):
    return lax.dot_general(
        left, right, (((0,), (0,)), ((), ())), precision=precision, preferred_element_type=jnp.float32
    )


def reduce_scatter(x, axes, n):
    chunks = x.reshape(n, x.shape[0] // n, *x.shape[1:])
    return lax.all_to_all(chunks, axes, 0, 0, tiled=False).sum(0)


def all_gather(piece, axes, n):
    copies = jnp.broadcast_to(piece[None], (n, *piece.shape))
    held = lax.all_to_all(copies, axes, 0, 0, tiled=False)
    return held.reshape(n * piece.shape[0], *piece.shape[1:])


def all_reduce(x, axes, n):
    copies = jnp.broadcast_to(x[None], (n, *x.shape))
    return lax.all_to_all(copies, axes, 0, 0, tiled=False).sum(0)


def unit_sum(x, stages):
    *outer, (last, n_last) = stages
    for axes, n in outer:
        x = reduce_scatter(x, axes, n)
    x = all_reduce(x, last, n_last)
    for axes, n in reversed(outer):
        x = all_gather(x, axes, n)
    return x


def samp_sum(x):
    return x + lax.ppermute(x, "samp", [(0, 1), (1, 0)])


def shards(stages, abundance, unitig_factor, sample_factor):
    unitig = unitig_factor
    sample = sample_factor
    n_samp = sample.shape[0]
    n_unit = unitig.shape[0]
    for sweep in range(ITERS):
        both = unit_sum(
            jnp.concatenate([inner(abundance, unitig, WIDE), inner(unitig, unitig)]), stages
        )
        target_h, gram_unit = both[:n_samp], both[n_samp:]
        sample = sample * target_h / jnp.dot(sample, gram_unit, precision=HI)
        both = samp_sum(
            jnp.concatenate([jnp.dot(abundance, sample, precision=WIDE), inner(sample, sample)])
        )
        target_w, gram_sample = both[:n_unit], both[n_unit:]
        unitig = unitig * target_w / jnp.dot(unitig, gram_sample, precision=HI)
    return (unitig, sample)


def unit_dims(mesh):
    row = mesh.devices[:, 0]
    n = row.shape[0]
    try:
        sizes = [len({d.coords[c] for d in row}) for c in (2, 1, 0)]
    except AttributeError:
        sizes = [n]
    if sizes[0] * sizes[1] * sizes[2] != n if len(sizes) == 3 else True:
        sizes = [n]
    names = ["uz", "uy", "ux"][: len(sizes)]
    return list(zip(names, sizes))


def stages_of(dims):
    if len(dims) < 3:
        return [(tuple(a for a, _ in dims), dims[0][1])]
    (z, nz), (y, ny), (x, nx) = dims
    return [((y, x), ny * nx), (z, nz)]


def solution(mesh):
    dims = unit_dims(mesh)
    inner_mesh = Mesh(
        mesh.devices.reshape(*[s for _, s in dims], mesh.devices.shape[1]),
        (*[a for a, _ in dims], "samp"),
    )
    unit = tuple(a for a, _ in dims)
    return jax.shard_map(
        lambda *args: shards(stages_of(dims), *args),
        mesh=inner_mesh,
        in_specs=(P(unit, "samp"), P(unit, None), P("samp", None)),
        out_specs=(P(unit, None), P("samp", None)),
        check_vma=False,
    )
```

```python
import jax
import jax.numpy as jnp
from jax import lax
from jax.sharding import Mesh
from jax.sharding import PartitionSpec as P

ITERS = 2


HI = lax.Precision.HIGH
WIDE = lax.Precision.HIGH


def inner(left, right, precision=HI):
    return lax.dot_general(
        left, right, (((0,), (0,)), ((), ())), precision=precision, preferred_element_type=jnp.float32
    )


def reduce_scatter(x, axes, n):
    chunks = x.reshape(n, x.shape[0] // n, *x.shape[1:])
    return lax.all_to_all(chunks, axes, 0, 0, tiled=False).sum(0)


def all_gather(piece, axes, n):
    copies = jnp.broadcast_to(piece[None], (n, *piece.shape))
    held = lax.all_to_all(copies, axes, 0, 0, tiled=False)
    return held.reshape(n * piece.shape[0], *piece.shape[1:])


def all_reduce(x, axes, n):
    copies = jnp.broadcast_to(x[None], (n, *x.shape))
    return lax.all_to_all(copies, axes, 0, 0, tiled=False).sum(0)


def unit_sum(x, stages):
    *outer, (last, n_last) = stages
    for axes, n in outer:
        x = reduce_scatter(x, axes, n)
    x = all_reduce(x, last, n_last)
    for axes, n in reversed(outer):
        x = all_gather(x, axes, n)
    return x


def samp_sum(x):
    return x + lax.ppermute(x, "samp", [(0, 1), (1, 0)])


def shards(stages, abundance, unitig_factor, sample_factor):
    unitig = unitig_factor
    sample = sample_factor
    n_samp = sample.shape[0]
    n_unit = unitig.shape[0]
    for sweep in range(ITERS):
        both = unit_sum(
            jnp.concatenate([inner(abundance, unitig, WIDE), inner(unitig, unitig)]), stages
        )
        target_h, gram_unit = both[:n_samp], both[n_samp:]
        sample = sample * target_h / jnp.dot(sample, gram_unit, precision=HI)
        both = samp_sum(
            jnp.concatenate([jnp.dot(abundance, sample, precision=WIDE), inner(sample, sample)])
        )
        target_w, gram_sample = both[:n_unit], both[n_unit:]
        unitig = unitig * target_w / jnp.dot(unitig, gram_sample, precision=HI)
    return (unitig, sample)


def unit_dims(mesh):
    row = mesh.devices[:, 0]
    n = row.shape[0]
    try:
        sizes = [len({d.coords[c] for d in row}) for c in (2, 1, 0)]
    except AttributeError:
        sizes = [n]
    if sizes[0] * sizes[1] * sizes[2] != n if len(sizes) == 3 else True:
        sizes = [n]
    names = ["uz", "uy", "ux"][: len(sizes)]
    return list(zip(names, sizes))


def stages_of(dims):
    if len(dims) < 3:
        return [(tuple(a for a, _ in dims), dims[0][1])]
    (z, nz), (y, ny), (x, nx) = dims
    return [((y, x), ny * nx), (z, nz)]


def solution(mesh):
    dims = unit_dims(mesh)
    inner_mesh = Mesh(
        mesh.devices.reshape(*[s for _, s in dims], mesh.devices.shape[1]),
        (*[a for a, _ in dims], "samp"),
    )
    unit = tuple(a for a, _ in dims)
    return jax.shard_map(
        lambda *args: shards(stages_of(dims), *args),
        mesh=inner_mesh,
        in_specs=(P(unit, "samp"), P(unit, None), P("samp", None)),
        out_specs=(P(unit, None), P("samp", None)),
        check_vma=False,
    )
```

```python
import jax
import jax.numpy as jnp
from jax import lax
from jax.sharding import Mesh
from jax.sharding import PartitionSpec as P

ITERS = 2


HI = lax.Precision.HIGH
WIDE = lax.Precision.HIGH


def inner(left, right, precision=HI):
    return lax.dot_general(
        left, right, (((0,), (0,)), ((), ())), precision=precision, preferred_element_type=jnp.float32
    )


def reduce_scatter(x, axes, n):
    chunks = x.reshape(n, x.shape[0] // n, *x.shape[1:])
    return lax.all_to_all(chunks, axes, 0, 0, tiled=False).sum(0)


def all_gather(piece, axes, n):
    copies = jnp.broadcast_to(piece[None], (n, *piece.shape))
    held = lax.all_to_all(copies, axes, 0, 0, tiled=False)
    return held.reshape(n * piece.shape[0], *piece.shape[1:])


def all_reduce(x, axes, n):
    copies = jnp.broadcast_to(x[None], (n, *x.shape))
    return lax.all_to_all(copies, axes, 0, 0, tiled=False).sum(0)


def unit_sum(x, stages):
    *outer, (last, n_last) = stages
    for axes, n in outer:
        x = reduce_scatter(x, axes, n)
    x = all_reduce(x, last, n_last)
    for axes, n in reversed(outer):
        x = all_gather(x, axes, n)
    return x


def samp_sum(x):
    return x + lax.ppermute(x, "samp", [(0, 1), (1, 0)])


def dot(spec, left, right):
    return jnp.einsum(spec, left, right, precision=HI, preferred_element_type=jnp.float32)


def shards(stages, abundance, unitig_factor, sample_factor):
    n = stages[0][1]
    rows, k = sample_factor.shape
    wide = abundance.reshape(abundance.shape[0], n, rows // n)
    unitig = unitig_factor.T
    sample = sample_factor.reshape(n, rows // n, k).transpose(0, 2, 1)
    for sweep in range(ITERS):
        gram_unit = dot("ku,lu->kl", unitig, unitig)
        target_h = dot("ku,ujs->jks", unitig, wide)
        width = rows // n
        both = jnp.concatenate([target_h, gram_unit.reshape(n, -1, width)], axis=1)
        both = unit_sum(both.reshape(-1, width), stages).reshape(n, -1, width)
        target_h, gram_unit = both[:, :k], both[:, k:].reshape(k, k)
        sample = sample * target_h / dot("kl,jks->jls", gram_unit, sample)
        gram_sample = dot("jks,jls->kl", sample, sample)
        both = samp_sum(jnp.concatenate([dot("jks,ujs->ku", sample, wide), gram_sample], axis=1))
        target_w, gram_sample = both[:, : unitig.shape[1]], both[:, unitig.shape[1] :]
        unitig = unitig * target_w / dot("kl,ku->lu", gram_sample, unitig)
    return (unitig.T, sample.transpose(0, 2, 1).reshape(rows, k))


def unit_dims(mesh):
    row = mesh.devices[:, 0]
    n = row.shape[0]
    try:
        sizes = [len({d.coords[c] for d in row}) for c in (2, 1, 0)]
    except AttributeError:
        sizes = [n]
    if sizes[0] * sizes[1] * sizes[2] != n if len(sizes) == 3 else True:
        sizes = [n]
    names = ["uz", "uy", "ux"][: len(sizes)]
    return list(zip(names, sizes))


def stages_of(dims):
    if len(dims) < 3:
        return [(tuple(a for a, _ in dims), dims[0][1])]
    (z, nz), (y, ny), (x, nx) = dims
    return [((y, x), ny * nx), (z, nz)]


def solution(mesh):
    dims = unit_dims(mesh)
    inner_mesh = Mesh(
        mesh.devices.reshape(*[s for _, s in dims], mesh.devices.shape[1]),
        (*[a for a, _ in dims], "samp"),
    )
    unit = tuple(a for a, _ in dims)
    return jax.shard_map(
        lambda *args: shards(stages_of(dims), *args),
        mesh=inner_mesh,
        in_specs=(P(unit, "samp"), P(unit, None), P("samp", None)),
        out_specs=(P(unit, None), P("samp", None)),
        check_vma=False,
    )
```

```python
import jax
import jax.numpy as jnp
from jax import lax
from jax.sharding import Mesh
from jax.sharding import PartitionSpec as P

ITERS = 2


HI = lax.Precision.HIGH
WIDE = lax.Precision.HIGH


def inner(left, right, precision=HI):
    return lax.dot_general(
        left, right, (((0,), (0,)), ((), ())), precision=precision, preferred_element_type=jnp.float32
    )


def reduce_scatter(x, axes, n):
    chunks = x.reshape(n, x.shape[0] // n, *x.shape[1:])
    return lax.all_to_all(chunks, axes, 0, 0, tiled=False).sum(0)


def all_gather(piece, axes, n):
    copies = jnp.broadcast_to(piece[None], (n, *piece.shape))
    held = lax.all_to_all(copies, axes, 0, 0, tiled=False)
    return held.reshape(n * piece.shape[0], *piece.shape[1:])


def all_reduce(x, axes, n):
    if n & (n - 1) == 0:
        d = 1
        while d < n:
            x = x + lax.ppermute(x, axes, [(j, j ^ d) for j in range(n)])
            d *= 2
        return x
    copies = jnp.broadcast_to(x[None], (n, *x.shape))
    return lax.all_to_all(copies, axes, 0, 0, tiled=False).sum(0)


def unit_sum(x, stages):
    *outer, (last, n_last) = stages
    for axes, n in outer:
        x = reduce_scatter(x, axes, n)
    x = all_reduce(x, last, n_last)
    for axes, n in reversed(outer):
        x = all_gather(x, axes, n)
    return x


def samp_sum(x):
    return x + lax.ppermute(x, "samp", [(0, 1), (1, 0)])


def dot(spec, left, right):
    return jnp.einsum(spec, left, right, precision=HI, preferred_element_type=jnp.float32)


def shards(stages, abundance, unitig_factor, sample_factor):
    n = stages[0][1]
    rows, k = sample_factor.shape
    wide = abundance.reshape(abundance.shape[0], n, rows // n)
    unitig = unitig_factor.T
    sample = sample_factor.reshape(n, rows // n, k).transpose(0, 2, 1)
    for sweep in range(ITERS):
        gram_unit = dot("ku,lu->kl", unitig, unitig)
        target_h = dot("ku,ujs->jks", unitig, wide)
        width = rows // n
        both = jnp.concatenate([target_h, gram_unit.reshape(n, -1, width)], axis=1)
        both = unit_sum(both.reshape(-1, width), stages).reshape(n, -1, width)
        target_h, gram_unit = both[:, :k], both[:, k:].reshape(k, k)
        sample = sample * target_h / dot("kl,jks->jls", gram_unit, sample)
        gram_sample = dot("jks,jls->kl", sample, sample)
        both = samp_sum(jnp.concatenate([dot("jks,ujs->ku", sample, wide), gram_sample], axis=1))
        target_w, gram_sample = both[:, : unitig.shape[1]], both[:, unitig.shape[1] :]
        unitig = unitig * target_w / dot("kl,ku->lu", gram_sample, unitig)
    return (unitig.T, sample.transpose(0, 2, 1).reshape(rows, k))


def unit_dims(mesh):
    row = mesh.devices[:, 0]
    n = row.shape[0]
    try:
        sizes = [len({d.coords[c] for d in row}) for c in (2, 1, 0)]
    except AttributeError:
        sizes = [n]
    if sizes[0] * sizes[1] * sizes[2] != n if len(sizes) == 3 else True:
        sizes = [n]
    names = ["uz", "uy", "ux"][: len(sizes)]
    return list(zip(names, sizes))


def stages_of(dims):
    if len(dims) < 3:
        return [(tuple(a for a, _ in dims), dims[0][1])]
    (z, nz), (y, ny), (x, nx) = dims
    return [((y, x), ny * nx), (z, nz)]


def solution(mesh):
    dims = unit_dims(mesh)
    inner_mesh = Mesh(
        mesh.devices.reshape(*[s for _, s in dims], mesh.devices.shape[1]),
        (*[a for a, _ in dims], "samp"),
    )
    unit = tuple(a for a, _ in dims)
    return jax.shard_map(
        lambda *args: shards(stages_of(dims), *args),
        mesh=inner_mesh,
        in_specs=(P(unit, "samp"), P(unit, None), P("samp", None)),
        out_specs=(P(unit, None), P("samp", None)),
        check_vma=False,
    )
```

```python
import jax
import jax.numpy as jnp
from jax import lax
from jax.sharding import Mesh
from jax.sharding import PartitionSpec as P

ITERS = 2


HI = lax.Precision.HIGH
WIDE = lax.Precision.HIGH


def inner(left, right, precision=HI):
    return lax.dot_general(
        left, right, (((0,), (0,)), ((), ())), precision=precision, preferred_element_type=jnp.float32
    )


def reduce_scatter(x, axes, n):
    chunks = x.reshape(n, x.shape[0] // n, *x.shape[1:])
    return lax.all_to_all(chunks, axes, 0, 0, tiled=False).sum(0)


def all_gather(piece, axes, n):
    copies = jnp.broadcast_to(piece[None], (n, *piece.shape))
    held = lax.all_to_all(copies, axes, 0, 0, tiled=False)
    return held.reshape(n * piece.shape[0], *piece.shape[1:])


def all_reduce(x, axes, n):
    if n % 2 == 0 and n >= 4:
        x = x + lax.ppermute(x, axes, [(j, j ^ 1) for j in range(n)])
        groups = n // 2
        mine = lax.axis_index(axes) // 2
        got = [x] + [
            lax.ppermute(x, axes, [(j, (((j // 2) ^ t) * 2) + j % 2) for j in range(n)])
            for t in range(1, groups)
        ]
        held = jnp.stack(got)
        ordered = jnp.take(held, jnp.arange(groups) ^ mine, axis=0)
        total = ordered[0]
        for g in range(1, groups):
            total = total + ordered[g]
        return total
    copies = jnp.broadcast_to(x[None], (n, *x.shape))
    return lax.all_to_all(copies, axes, 0, 0, tiled=False).sum(0)


def unit_sum(x, stages):
    *outer, (last, n_last) = stages
    for axes, n in outer:
        x = reduce_scatter(x, axes, n)
    x = all_reduce(x, last, n_last)
    for axes, n in reversed(outer):
        x = all_gather(x, axes, n)
    return x


def samp_sum(x):
    return x + lax.ppermute(x, "samp", [(0, 1), (1, 0)])


def dot(spec, left, right):
    return jnp.einsum(spec, left, right, precision=HI, preferred_element_type=jnp.float32)


def shards(stages, abundance, unitig_factor, sample_factor):
    n = stages[0][1]
    rows, k = sample_factor.shape
    wide = abundance.reshape(abundance.shape[0], n, rows // n)
    unitig = unitig_factor.T
    sample = sample_factor.reshape(n, rows // n, k).transpose(0, 2, 1)
    for sweep in range(ITERS):
        gram_unit = dot("ku,lu->kl", unitig, unitig)
        target_h = dot("ku,ujs->jks", unitig, wide)
        width = rows // n
        both = jnp.concatenate([target_h, gram_unit.reshape(n, -1, width)], axis=1)
        both = unit_sum(both.reshape(-1, width), stages).reshape(n, -1, width)
        target_h, gram_unit = both[:, :k], both[:, k:].reshape(k, k)
        sample = sample * target_h / dot("kl,jks->jls", gram_unit, sample)
        gram_sample = dot("jks,jls->kl", sample, sample)
        both = samp_sum(jnp.concatenate([dot("jks,ujs->ku", sample, wide), gram_sample], axis=1))
        target_w, gram_sample = both[:, : unitig.shape[1]], both[:, unitig.shape[1] :]
        unitig = unitig * target_w / dot("kl,ku->lu", gram_sample, unitig)
    return (unitig.T, sample.transpose(0, 2, 1).reshape(rows, k))


def unit_dims(mesh):
    row = mesh.devices[:, 0]
    n = row.shape[0]
    try:
        sizes = [len({d.coords[c] for d in row}) for c in (2, 1, 0)]
    except AttributeError:
        sizes = [n]
    if sizes[0] * sizes[1] * sizes[2] != n if len(sizes) == 3 else True:
        sizes = [n]
    names = ["uz", "uy", "ux"][: len(sizes)]
    return list(zip(names, sizes))


def stages_of(dims):
    if len(dims) < 3:
        return [(tuple(a for a, _ in dims), dims[0][1])]
    (z, nz), (y, ny), (x, nx) = dims
    return [((y, x), ny * nx), (z, nz)]


def solution(mesh):
    dims = unit_dims(mesh)
    inner_mesh = Mesh(
        mesh.devices.reshape(*[s for _, s in dims], mesh.devices.shape[1]),
        (*[a for a, _ in dims], "samp"),
    )
    unit = tuple(a for a, _ in dims)
    return jax.shard_map(
        lambda *args: shards(stages_of(dims), *args),
        mesh=inner_mesh,
        in_specs=(P(unit, "samp"), P(unit, None), P("samp", None)),
        out_specs=(P(unit, None), P("samp", None)),
        check_vma=False,
    )
```

```python
import jax
import jax.numpy as jnp
from jax import lax
from jax.sharding import Mesh
from jax.sharding import PartitionSpec as P

ITERS = 2


HI = lax.Precision.HIGH
WIDE = lax.Precision.HIGH


def inner(left, right, precision=HI):
    return lax.dot_general(
        left, right, (((0,), (0,)), ((), ())), precision=precision, preferred_element_type=jnp.float32
    )


def reduce_scatter(x, axes, n):
    chunks = x.reshape(n, x.shape[0] // n, *x.shape[1:])
    return lax.all_to_all(chunks, axes, 0, 0, tiled=False).sum(0)


def all_gather(piece, axes, n):
    copies = jnp.broadcast_to(piece[None], (n, *piece.shape))
    held = lax.all_to_all(copies, axes, 0, 0, tiled=False)
    return held.reshape(n * piece.shape[0], *piece.shape[1:])


def all_reduce(x, axes, n):
    if n & (n - 1) == 0:
        d = n // 2
        while d >= 1:
            x = x + lax.ppermute(x, axes, [(j, j ^ d) for j in range(n)])
            d //= 2
        return x
    copies = jnp.broadcast_to(x[None], (n, *x.shape))
    return lax.all_to_all(copies, axes, 0, 0, tiled=False).sum(0)


def unit_sum(x, stages):
    *outer, (last, n_last) = stages
    for axes, n in outer:
        x = reduce_scatter(x, axes, n)
    x = all_reduce(x, last, n_last)
    for axes, n in reversed(outer):
        x = all_gather(x, axes, n)
    return x


def samp_sum(x):
    return x + lax.ppermute(x, "samp", [(0, 1), (1, 0)])


def dot(spec, left, right):
    return jnp.einsum(spec, left, right, precision=HI, preferred_element_type=jnp.float32)


def shards(stages, abundance, unitig_factor, sample_factor):
    n = stages[0][1]
    rows, k = sample_factor.shape
    wide = abundance.reshape(abundance.shape[0], n, rows // n)
    unitig = unitig_factor.T
    sample = sample_factor.reshape(n, rows // n, k).transpose(0, 2, 1)
    for sweep in range(ITERS):
        gram_unit = dot("ku,lu->kl", unitig, unitig)
        target_h = dot("ku,ujs->jks", unitig, wide)
        width = rows // n
        both = jnp.concatenate([target_h, gram_unit.reshape(n, -1, width)], axis=1)
        both = unit_sum(both.reshape(-1, width), stages).reshape(n, -1, width)
        target_h, gram_unit = both[:, :k], both[:, k:].reshape(k, k)
        sample = sample * target_h / dot("kl,jks->jls", gram_unit, sample)
        gram_sample = dot("jks,jls->kl", sample, sample)
        both = samp_sum(jnp.concatenate([dot("jks,ujs->ku", sample, wide), gram_sample], axis=1))
        target_w, gram_sample = both[:, : unitig.shape[1]], both[:, unitig.shape[1] :]
        unitig = unitig * target_w / dot("kl,ku->lu", gram_sample, unitig)
    return (unitig.T, sample.transpose(0, 2, 1).reshape(rows, k))


def unit_dims(mesh):
    row = mesh.devices[:, 0]
    n = row.shape[0]
    try:
        sizes = [len({d.coords[c] for d in row}) for c in (2, 1, 0)]
    except AttributeError:
        sizes = [n]
    if sizes[0] * sizes[1] * sizes[2] != n if len(sizes) == 3 else True:
        sizes = [n]
    names = ["uz", "uy", "ux"][: len(sizes)]
    return list(zip(names, sizes))


def stages_of(dims):
    if len(dims) < 3:
        return [(tuple(a for a, _ in dims), dims[0][1])]
    (z, nz), (y, ny), (x, nx) = dims
    return [((y, x), ny * nx), (z, nz)]


def solution(mesh):
    dims = unit_dims(mesh)
    inner_mesh = Mesh(
        mesh.devices.reshape(*[s for _, s in dims], mesh.devices.shape[1]),
        (*[a for a, _ in dims], "samp"),
    )
    unit = tuple(a for a, _ in dims)
    return jax.shard_map(
        lambda *args: shards(stages_of(dims), *args),
        mesh=inner_mesh,
        in_specs=(P(unit, "samp"), P(unit, None), P("samp", None)),
        out_specs=(P(unit, None), P("samp", None)),
        check_vma=False,
    )
```

```python
import jax
import jax.numpy as jnp
from jax import lax
from jax.sharding import Mesh
from jax.sharding import PartitionSpec as P

ITERS = 2


HI = lax.Precision.HIGH
WIDE = lax.Precision.HIGH


def inner(left, right, precision=HI):
    return lax.dot_general(
        left, right, (((0,), (0,)), ((), ())), precision=precision, preferred_element_type=jnp.float32
    )


def reduce_scatter(x, axes, n):
    chunks = x.reshape(n, x.shape[0] // n, *x.shape[1:])
    return lax.all_to_all(chunks, axes, 0, 0, tiled=False).sum(0)


def all_gather(piece, axes, n):
    copies = jnp.broadcast_to(piece[None], (n, *piece.shape))
    held = lax.all_to_all(copies, axes, 0, 0, tiled=False)
    return held.reshape(n * piece.shape[0], *piece.shape[1:])


def all_reduce(x, axes, n):
    if n & (n - 1) == 0:
        d = 1
        while d < n:
            x = x + lax.ppermute(x, axes, [(j, j ^ d) for j in range(n)])
            d *= 2
        return x
    copies = jnp.broadcast_to(x[None], (n, *x.shape))
    return lax.all_to_all(copies, axes, 0, 0, tiled=False).sum(0)


def unit_sum(x, stages, own=lambda piece: piece):
    *outer, (last, n_last) = stages
    for axes, n in outer:
        x = reduce_scatter(x, axes, n)
    x = own(all_reduce(x, last, n_last))
    for axes, n in reversed(outer):
        x = all_gather(x, axes, n)
    return x


def samp_sum(x):
    return x + lax.ppermute(x, "samp", [(0, 1), (1, 0)])


def dot(spec, left, right):
    return jnp.einsum(spec, left, right, precision=HI, preferred_element_type=jnp.float32)


def shards(stages, abundance, unitig_factor, sample_factor):
    n = stages[0][1]
    rows, k = sample_factor.shape
    wide = abundance.reshape(abundance.shape[0], n, rows // n)
    unitig = unitig_factor.T
    sample = sample_factor.reshape(n, rows // n, k).transpose(0, 2, 1)
    for sweep in range(ITERS):
        gram_unit = dot("ku,lu->kl", unitig, unitig)
        target_h = dot("ku,ujs->jks", unitig, wide)
        width = rows // n
        both = jnp.concatenate([target_h, gram_unit.reshape(n, -1, width)], axis=1)
        if width == k:
            turn = lambda piece: jnp.concatenate([piece[:k].T, piece[k:]])
            both = unit_sum(both.reshape(-1, width), stages, turn).reshape(n, -1, width)
            target_h = both[:, :k].transpose(0, 2, 1)
        else:
            both = unit_sum(both.reshape(-1, width), stages).reshape(n, -1, width)
            target_h = both[:, :k]
        gram_unit = both[:, k:].reshape(k, k)
        sample = sample * target_h / dot("kl,jks->jls", gram_unit, sample)
        gram_sample = dot("jks,jls->kl", sample, sample)
        both = samp_sum(jnp.concatenate([dot("jks,ujs->ku", sample, wide), gram_sample], axis=1))
        target_w, gram_sample = both[:, : unitig.shape[1]], both[:, unitig.shape[1] :]
        unitig = unitig * target_w / dot("kl,ku->lu", gram_sample, unitig)
    return (unitig.T, sample.transpose(0, 2, 1).reshape(rows, k))


def unit_dims(mesh):
    row = mesh.devices[:, 0]
    n = row.shape[0]
    try:
        sizes = [len({d.coords[c] for d in row}) for c in (2, 1, 0)]
    except AttributeError:
        sizes = [n]
    if sizes[0] * sizes[1] * sizes[2] != n if len(sizes) == 3 else True:
        sizes = [n]
    names = ["uz", "uy", "ux"][: len(sizes)]
    return list(zip(names, sizes))


def stages_of(dims):
    if len(dims) < 3:
        return [(tuple(a for a, _ in dims), dims[0][1])]
    (z, nz), (y, ny), (x, nx) = dims
    return [((y, x), ny * nx), (z, nz)]


def solution(mesh):
    dims = unit_dims(mesh)
    inner_mesh = Mesh(
        mesh.devices.reshape(*[s for _, s in dims], mesh.devices.shape[1]),
        (*[a for a, _ in dims], "samp"),
    )
    unit = tuple(a for a, _ in dims)
    return jax.shard_map(
        lambda *args: shards(stages_of(dims), *args),
        mesh=inner_mesh,
        in_specs=(P(unit, "samp"), P(unit, None), P("samp", None)),
        out_specs=(P(unit, None), P("samp", None)),
        check_vma=False,
    )
```

```python
import jax
import jax.numpy as jnp
from jax import lax
from jax.sharding import Mesh
from jax.sharding import PartitionSpec as P

ITERS = 2


HI = lax.Precision.HIGH
WIDE = lax.Precision.HIGH


def inner(left, right, precision=HI):
    return lax.dot_general(
        left, right, (((0,), (0,)), ((), ())), precision=precision, preferred_element_type=jnp.float32
    )


def reduce_scatter(x, axes, n):
    chunks = x.reshape(n, x.shape[0] // n, *x.shape[1:])
    return lax.all_to_all(chunks, axes, 0, 0, tiled=False).sum(0)


def all_gather(piece, axes, n):
    copies = jnp.broadcast_to(piece[None], (n, *piece.shape))
    held = lax.all_to_all(copies, axes, 0, 0, tiled=False)
    return held.reshape(n * piece.shape[0], *piece.shape[1:])


def all_reduce(x, axes, n):
    if n & (n - 1) == 0:
        d = 1
        while d < n:
            x = x + lax.ppermute(x, axes, [(j, j ^ d) for j in range(n)])
            d *= 2
        return x
    copies = jnp.broadcast_to(x[None], (n, *x.shape))
    return lax.all_to_all(copies, axes, 0, 0, tiled=False).sum(0)


def unit_sum(x, stages, own=lambda piece: piece):
    *outer, (last, n_last) = stages
    for axes, n in outer:
        x = reduce_scatter(x, axes, n)
    x = own(all_reduce(x, last, n_last))
    for axes, n in reversed(outer):
        x = all_gather(x, axes, n)
    return x


def samp_sum(x):
    return x + lax.ppermute(x, "samp", [(0, 1), (1, 0)])


def dot(spec, left, right):
    return jnp.einsum(spec, left, right, precision=HI, preferred_element_type=jnp.float32)


def shards(stages, abundance, unitig_factor, sample_factor):
    n = stages[0][1]
    rows, k = sample_factor.shape
    wide = abundance.reshape(abundance.shape[0], n, rows // n)
    unitig = lax.optimization_barrier(unitig_factor.T)
    sample = sample_factor.reshape(n, rows // n, k).transpose(0, 2, 1)
    for sweep in range(ITERS):
        gram_unit = dot("ku,lu->kl", unitig, unitig)
        target_h = dot("ku,ujs->jks", unitig, wide)
        width = rows // n
        both = jnp.concatenate([target_h, gram_unit.reshape(n, -1, width)], axis=1)
        if width == k:
            turn = lambda piece: jnp.concatenate([piece[:k].T, piece[k:]])
            both = unit_sum(both.reshape(-1, width), stages, turn).reshape(n, -1, width)
            target_h = both[:, :k].transpose(0, 2, 1)
        else:
            both = unit_sum(both.reshape(-1, width), stages).reshape(n, -1, width)
            target_h = both[:, :k]
        gram_unit = both[:, k:].reshape(k, k)
        sample = sample * target_h / dot("kl,jks->jls", gram_unit, sample)
        gram_sample = dot("jks,jls->kl", sample, sample)
        both = samp_sum(jnp.concatenate([dot("jks,ujs->ku", sample, wide), gram_sample], axis=1))
        target_w, gram_sample = both[:, : unitig.shape[1]], both[:, unitig.shape[1] :]
        unitig = unitig * target_w / dot("kl,ku->lu", gram_sample, unitig)
    return (unitig.T, sample.transpose(0, 2, 1).reshape(rows, k))


def unit_dims(mesh):
    row = mesh.devices[:, 0]
    n = row.shape[0]
    try:
        sizes = [len({d.coords[c] for d in row}) for c in (2, 1, 0)]
    except AttributeError:
        sizes = [n]
    if sizes[0] * sizes[1] * sizes[2] != n if len(sizes) == 3 else True:
        sizes = [n]
    names = ["uz", "uy", "ux"][: len(sizes)]
    return list(zip(names, sizes))


def stages_of(dims):
    if len(dims) < 3:
        return [(tuple(a for a, _ in dims), dims[0][1])]
    (z, nz), (y, ny), (x, nx) = dims
    return [((y, x), ny * nx), (z, nz)]


def solution(mesh):
    dims = unit_dims(mesh)
    inner_mesh = Mesh(
        mesh.devices.reshape(*[s for _, s in dims], mesh.devices.shape[1]),
        (*[a for a, _ in dims], "samp"),
    )
    unit = tuple(a for a, _ in dims)
    return jax.shard_map(
        lambda *args: shards(stages_of(dims), *args),
        mesh=inner_mesh,
        in_specs=(P(unit, "samp"), P(unit, None), P("samp", None)),
        out_specs=(P(unit, None), P("samp", None)),
        check_vma=False,
    )
```
